256 devices in a mesh: row: 16 (over y_hi, x, core), col: 16 (over z, y_lo).
Axes of the slice: x: 4, y: 4 (y_hi: 2, y_lo: 2; y = y_hi * 2 + y_lo), z: 8, core: 2. Of those that a mesh axis runs over, the one named last changes fastest.
Arguments:
- inputs: bfloat16 [1024, 16384], P('col', 'row'), may hold values from -6 to 6
- out_grad: bfloat16 [1024, 16384], P('col', 'row'), may hold values from -0.1875 to 0.1875
- states: bfloat16 [16384, 1024], P(('col', 'row')), may hold values from -6 to 6
- in_weight: bfloat16 [16384, 16384], P('row', 'col'), may hold values from -0.046875 to 0.046875
- out_weight: bfloat16 [16384, 16384], P('col', 'row'), may hold values from -0.046875 to 0.046875
- decay_rate: float32 [4, 16384], P(None, ('col', 'row')), may hold values from 0.0015625 to 0.1
- session_ids: int32 [4], replicated, may hold values from 0 to 3, each once
- lengths: int32 [4], replicated, may hold values from 1 to 256, 640 in all
Outputs:
- input_grad: bfloat16 [1024, 16384], P('col', 'row')
- in_weight_grad: bfloat16 [16384, 16384], P('row', 'col')
- out_weight_grad: bfloat16 [16384, 16384], P('col', 'row')
- rate_grad: float32 [4, 16384], P(None, ('col', 'row'))
The draws below stay inside these ranges and needn't reach their ends.
Inputs may be any that keep to these rules, and one draw needn't show every extreme that they name: `session_ids`: each session appears in exactly one sequence. The lengths sum to 640.
All inputs are finite; a program needn't handle non-finite values.
Results may differ from the reference program's by a relative error of at most 0.024.
Values may be sent and summed in bfloat16 or wider, within the bound.
No kernel may reach another device: no remote copies, remote signals or barrier semaphores. Data moves between devices by JAX's collectives and lax.ppermute only.
A program may use at most 128 MiB of HBM per device.

```python
import math
import jax
import jax.numpy as jnp
import numpy as np
from jax import lax

D = 16384
H = 16384
L = 256
SEQ = 4
SESSIONS = 4
TOKENS = 1024
N_ROW = 16
N_COL = 16


def level_of(stream_key, dims, pieces, least, high):
    factor_of = 1.0
    for dim, parts in pieces:
        steps = jax.random.uniform(jax.random.fold_in(jax.random.fold_in(stream_key, 6), dim), (parts,), jnp.float32, least / len(pieces), high / len(pieces))
        factor_of = factor_of * jnp.repeat(jnp.exp(steps), dims[dim] // parts).reshape((-1,) + (1,) * (len(dims) - 1 - dim))
    return factor_of


def profile(count, total, reach, skew):
    weights = [(1 << 20) // math.isqrt(standing ** skew) + 1 for standing in range(2, count + 1)]
    rest, counts = total - reach - (count - 1), [1] * (count - 1)
    while rest > 0:
        candidates = [i for i in range(count - 1) if counts[i] < reach]
        whole, remaining = sum([weights[i] for i in candidates]), rest
        for i in candidates:
            addition = min(reach - counts[i], max(1, remaining * weights[i] // whole), rest)
            counts[i] = counts[i] + addition
            rest = rest - addition
    return np.array([reach] + counts)


def ragged_sizes(rng, count, total, bound, slope):
    if count == 2:
        one = jax.random.randint(rng, (), max(1, total - bound), min(bound, total - 1) + 1)
        return jnp.stack([one, total - one])
    sizes = jnp.asarray(profile(count, total, bound, slope), jnp.int32)
    couples = (count - 1) // 2
    donor, sink = sizes[1:1 + 2 * couples:2], sizes[2:2 + 2 * couples:2]
    margin = jnp.minimum(donor - 1, bound - sink)
    shifted = jax.random.randint(jax.random.fold_in(rng, 1), (couples,), 0, 1 << 20) % (margin + 1)
    sizes = sizes.at[1:1 + 2 * couples:2].set(donor - shifted).at[2:2 + 2 * couples:2].set(sink + shifted)
    return sizes[jax.random.permutation(jax.random.fold_in(rng, 2), count)]


def gaussian(own_key, extent, deviation, most, split=(), held_as=jnp.bfloat16):
    factor_of = level_of(own_key, extent, split, -0.22, 0.18) if split else 1.0
    array = jax.random.normal(own_key, extent, jnp.float32) * deviation * factor_of
    return jnp.minimum(jnp.maximum(array, -most), most).astype(held_as)


def setup_inputs(seed: int = 0) -> dict:
    splits = jax.random.split(jax.random.key(seed), 9)
    inputs = gaussian(splits[0], (TOKENS, D), 1.0, 6.0, ((0, 16), (1, 16)))
    out_grad = gaussian(splits[1], (TOKENS, D), (1.0 / TOKENS ** 0.5), 0.1875, ((0, 16), (1, 16)))
    states = gaussian(splits[2], (H, TOKENS), 1.0, 6.0, ((0, 256),))
    in_weight = gaussian(splits[3], (D, H), D ** -0.5, 0.046875, ((0, 16), (1, 16)))
    out_weight = gaussian(splits[4], (H, D), H ** -0.5, 0.046875, ((0, 16), (1, 16)))
    decay_rate = jnp.clip(jnp.exp(math.log(0.1) - 4.158883 * jax.random.uniform(splits[5], (SESSIONS, H), jnp.float32) ** level_of(splits[5], (SESSIONS, H), ((1, 256),), -0.2, 0.2)), 0.0015625, 0.1)
    session_ids = jax.random.permutation(splits[6], SEQ).astype(jnp.int32)
    lengths = ragged_sizes(splits[7], SEQ, L + (SEQ - 1) * L // 2, L, 1).astype(jnp.int32)
    return {"inputs": inputs, "out_grad": out_grad, "states": states, "in_weight": in_weight, "out_weight": out_weight, "decay_rate": decay_rate, "session_ids": session_ids, "lengths": lengths}


def reference(inputs, out_grad, states, in_weight, out_weight, decay_rate, session_ids, lengths):
    position = jnp.arange(TOKENS, dtype=jnp.int32) % L
    seq_index = jnp.arange(TOKENS, dtype=jnp.int32) // L
    valid_bin = position >= L - lengths[seq_index]
    masked = jnp.where(valid_bin[:, None], out_grad, jnp.zeros_like(out_grad))
    feature_part = D // N_ROW
    state_grad = jnp.zeros((H, TOKENS), jnp.float32)
    for index in range(N_ROW):
        columns = slice(index * feature_part, (index + 1) * feature_part)
        partial_value = lax.dot_general(out_weight[:, columns], masked[:, columns], (((1,), (1,)), ((), ())), preferred_element_type=jnp.float32)
        rounded = lax.optimization_barrier(partial_value.astype(jnp.bfloat16))
        state_grad = state_grad + rounded.astype(jnp.float32)
    decays = 1.0 - decay_rate[session_ids].T
    grad_seq = state_grad.reshape(H, SEQ, L)

    def backstep(carried, column):
        updated = column + decays * carried
        return updated, updated

    _, swept = lax.scan(backstep, jnp.zeros((H, SEQ), jnp.float32), jnp.moveaxis(grad_seq, 2, 0), reverse=True)
    adjoint = jnp.moveaxis(swept, 0, 2)
    previous = states.astype(jnp.float32).reshape(H, SEQ, L)
    per_seq = jnp.sum(adjoint[:, :, 1:] * previous[:, :, :-1], axis=2)
    rate_grad = jnp.zeros((SESSIONS, H), jnp.float32).at[session_ids].add(-per_seq.T)
    state_in = adjoint.reshape(H, TOKENS).astype(jnp.bfloat16)
    out_weight_grad = jnp.dot(states, masked, preferred_element_type=jnp.float32).astype(jnp.bfloat16)
    in_weight_grad = lax.dot_general(inputs, state_in, (((0,), (1,)), ((), ())), preferred_element_type=jnp.float32).astype(jnp.bfloat16)
    channel_part = H // N_COL
    running = jnp.zeros((TOKENS, D), jnp.float32)
    for index in range(N_COL):
        channels = slice(index * channel_part, (index + 1) * channel_part)
        partial_value = lax.dot_general(state_in[channels], in_weight[:, channels], (((0,), (1,)), ((), ())), preferred_element_type=jnp.float32)
        rounded = lax.optimization_barrier(partial_value.astype(jnp.bfloat16))
        running = running + rounded.astype(jnp.float32)
    input_grad = running.astype(jnp.bfloat16)
    return input_grad, in_weight_grad, out_weight_grad, rate_grad
```

```python
import jax
import jax.numpy as jnp
from jax import lax
from jax.sharding import PartitionSpec as P

exact_mode = lax.Precision.HIGHEST


def contract(left_side, right_side, left_dim, right_dim):
    return lax.dot_general(
        left_side,
        right_side,
        (((left_dim,), (right_dim,)), ((), ())),
        preferred_element_type=jnp.float32,
    )


def session_table(session_ids, table_rows):
    return (session_ids[:, None] == jnp.arange(table_rows, dtype=jnp.int32)[None, :]).astype(
        jnp.float32
    )


def gather_rows(share, axis_name, parts):
    spread = jnp.broadcast_to(share[None], (parts,) + share.shape)
    return lax.all_to_all(spread, axis_name, 0, 0).reshape((-1,) + share.shape[1:])


def scatter_sum(partial, axis_name, parts):
    pieces = lax.all_to_all(partial.reshape((parts, -1) + partial.shape[1:]), axis_name, 0, 0)
    return jnp.sum(pieces.astype(jnp.float32), axis=0)


def adjoint_sweep(state_grad, rate_rows, onehot, seq_count):
    channels = state_grad.shape[0]
    seq_rate = jnp.dot(onehot, rate_rows, precision=exact_mode)
    decays = (1.0 - seq_rate).T
    running = state_grad.reshape(channels, seq_count, -1)
    bins = running.shape[2]
    factor = decays[:, :, None]
    shift = 1
    while shift < bins:
        ahead = jnp.concatenate(
            [running[:, :, shift:], jnp.zeros((channels, seq_count, shift), running.dtype)], axis=2
        )
        running = running + factor * ahead
        factor = factor * factor
        shift *= 2
    return running.reshape(channels, -1)


def rate_term(adjoint, states_share, onehot, seq_count):
    channels = adjoint.shape[0]
    adjoint_seq = adjoint.reshape(channels, seq_count, -1)
    previous = states_share.astype(jnp.float32).reshape(channels, seq_count, -1)
    per_seq = jnp.sum(adjoint_seq[:, :, 1:] * previous[:, :, :-1], axis=2)
    return -jnp.dot(onehot.T, per_seq.T, precision=exact_mode)


def per_device(inputs, out_grad, states, in_weight, out_weight, decay_rate, session_ids, lengths):
    n_row = lax.axis_size("row")
    n_col = lax.axis_size("col")
    seq_count = session_ids.shape[0]
    onehot = session_table(session_ids, decay_rate.shape[0])
    grad_rows = gather_rows(out_grad, "col", n_col)
    token_total = grad_rows.shape[0]
    bin_count = token_total // seq_count
    token_ids = jnp.arange(token_total, dtype=jnp.int32)
    seq_match = (token_ids // bin_count)[:, None] == jnp.arange(seq_count, dtype=jnp.int32)[None, :]
    seq_length = jnp.sum(jnp.where(seq_match, lengths[None, :], 0), axis=1)
    valid_bin = token_ids % bin_count >= bin_count - seq_length
    masked = jnp.where(valid_bin[:, None], grad_rows, jnp.zeros_like(grad_rows))
    state_grad = scatter_sum(contract(out_weight, masked, 1, 1).astype(jnp.bfloat16), "row", n_row)
    states_rows = gather_rows(states, "row", n_row)
    out_weight_grad = jnp.dot(states_rows, masked, preferred_element_type=jnp.float32).astype(
        jnp.bfloat16
    )
    adjoint = adjoint_sweep(state_grad, decay_rate, onehot, seq_count)
    rate_grad = rate_term(adjoint, states, onehot, seq_count)
    gathered = gather_rows(adjoint.astype(jnp.bfloat16), "row", n_row)
    input_rows = gather_rows(inputs, "col", n_col)
    in_weight_grad = contract(input_rows, gathered, 0, 1).astype(jnp.bfloat16)
    input_grad = scatter_sum(
        contract(gathered, in_weight, 0, 1).astype(jnp.bfloat16), "col", n_col
    ).astype(jnp.bfloat16)
    return (input_grad, in_weight_grad, out_weight_grad, rate_grad)


def solution(mesh):
    return jax.shard_map(
        per_device,
        mesh=mesh,
        in_specs=(
            P("col", "row"),
            P("col", "row"),
            P(("col", "row"), None),
            P("row", "col"),
            P("col", "row"),
            P(None, ("col", "row")),
            P(),
            P(),
        ),
        out_specs=(P("col", "row"), P("row", "col"), P("col", "row"), P(None, ("col", "row"))),
        check_vma=False,
    )
```

```python
import jax
import jax.numpy as jnp
from jax import lax
from jax.sharding import PartitionSpec as P

exact_mode = lax.Precision.HIGHEST


def contract(left_side, right_side, left_dim, right_dim):
    return lax.dot_general(
        left_side,
        right_side,
        (((left_dim,), (right_dim,)), ((), ())),
        preferred_element_type=jnp.float32,
    )


def session_table(session_ids, table_rows):
    return (session_ids[:, None] == jnp.arange(table_rows, dtype=jnp.int32)[None, :]).astype(
        jnp.float32
    )


def gather_rows(share, axis_name, parts):
    spread = jnp.broadcast_to(share[None], (parts,) + share.shape)
    return lax.all_to_all(spread, axis_name, 0, 0).reshape((-1,) + share.shape[1:])


def scatter_sum(partial, axis_name, parts):
    pieces = lax.all_to_all(partial.reshape((parts, -1) + partial.shape[1:]), axis_name, 0, 0)
    return jnp.sum(pieces.astype(jnp.float32), axis=0)


def adjoint_sweep(state_grad, rate_rows, onehot, seq_count):
    channels = state_grad.shape[0]
    seq_rate = jnp.dot(onehot, rate_rows, precision=exact_mode)
    decays = (1.0 - seq_rate).T
    running = state_grad.reshape(channels, seq_count, -1)
    bins = running.shape[2]
    factor = decays[:, :, None]
    shift = 1
    while shift < bins:
        ahead = jnp.concatenate(
            [running[:, :, shift:], jnp.zeros((channels, seq_count, shift), running.dtype)], axis=2
        )
        running = running + factor * ahead
        factor = factor * factor
        shift *= 2
    return running.reshape(channels, -1)


def rate_term(adjoint, states_share, onehot, seq_count):
    channels = adjoint.shape[0]
    adjoint_seq = adjoint.reshape(channels, seq_count, -1)
    previous = states_share.astype(jnp.float32).reshape(channels, seq_count, -1)
    per_seq = jnp.sum(adjoint_seq[:, :, 1:] * previous[:, :, :-1], axis=2)
    return -jnp.dot(onehot.T, per_seq.T, precision=exact_mode)


def per_device(inputs, out_grad, states, in_weight, out_weight, decay_rate, session_ids, lengths):
    n_row = lax.axis_size("row")
    n_col = lax.axis_size("col")
    seq_count = session_ids.shape[0]
    onehot = session_table(session_ids, decay_rate.shape[0])
    grad_rows = gather_rows(out_grad, "col", n_col)
    token_total = grad_rows.shape[0]
    bin_count = token_total // seq_count
    token_ids = jnp.arange(token_total, dtype=jnp.int32)
    seq_match = (token_ids // bin_count)[:, None] == jnp.arange(seq_count, dtype=jnp.int32)[None, :]
    seq_length = jnp.sum(jnp.where(seq_match, lengths[None, :], 0), axis=1)
    valid_bin = token_ids % bin_count >= bin_count - seq_length
    masked = jnp.where(valid_bin[:, None], grad_rows, jnp.zeros_like(grad_rows))
    state_grad = scatter_sum(contract(out_weight, masked, 1, 1).astype(jnp.bfloat16), "row", n_row)
    states_rows = lax.all_gather(states, "row", axis=0, tiled=True)
    out_weight_grad = jnp.dot(states_rows, masked, preferred_element_type=jnp.float32).astype(
        jnp.bfloat16
    )
    adjoint = adjoint_sweep(state_grad, decay_rate, onehot, seq_count)
    rate_grad = rate_term(adjoint, states, onehot, seq_count)
    gathered = gather_rows(adjoint.astype(jnp.bfloat16), "row", n_row)
    input_rows = lax.all_gather(inputs, "col", axis=0, tiled=True)
    in_weight_grad = contract(input_rows, gathered, 0, 1).astype(jnp.bfloat16)
    input_grad = scatter_sum(
        contract(gathered, in_weight, 0, 1).astype(jnp.bfloat16), "col", n_col
    ).astype(jnp.bfloat16)
    return (input_grad, in_weight_grad, out_weight_grad, rate_grad)


def solution(mesh):
    return jax.shard_map(
        per_device,
        mesh=mesh,
        in_specs=(
            P("col", "row"),
            P("col", "row"),
            P(("col", "row"), None),
            P("row", "col"),
            P("col", "row"),
            P(None, ("col", "row")),
            P(),
            P(),
        ),
        out_specs=(P("col", "row"), P("row", "col"), P("col", "row"), P(None, ("col", "row"))),
        check_vma=False,
    )
```

```python
import jax
import jax.numpy as jnp
from jax import lax
from jax.sharding import Mesh, PartitionSpec as P

exact_mode = lax.Precision.HIGHEST


def contract(left_side, right_side, left_dim, right_dim):
    return lax.dot_general(
        left_side,
        right_side,
        (((left_dim,), (right_dim,)), ((), ())),
        preferred_element_type=jnp.float32,
    )


def session_table(session_ids, table_rows):
    return (session_ids[:, None] == jnp.arange(table_rows, dtype=jnp.int32)[None, :]).astype(
        jnp.float32
    )


def gather_rows(share, axis_name, parts):
    spread = jnp.broadcast_to(share[None], (parts,) + share.shape)
    return lax.all_to_all(spread, axis_name, 0, 0).reshape((-1,) + share.shape[1:])


def scatter_sum(partial, axis_name, parts):
    pieces = lax.all_to_all(partial.reshape((parts, -1) + partial.shape[1:]), axis_name, 0, 0)
    return jnp.sum(pieces.astype(jnp.float32), axis=0)


def gather_channels(share):
    core = lax.axis_index("core")
    chips = lax.axis_size("rchip")
    mine = gather_rows(share, "rchip", chips).reshape((chips, 1) + share.shape)
    other = lax.ppermute(mine, "core", [(0, 1), (1, 0)])
    ordered = jnp.where(core == 0, jnp.concatenate([mine, other], 1), jnp.concatenate([other, mine], 1))
    return ordered.reshape((-1,) + share.shape[1:])


def scatter_channels(partial):
    core = lax.axis_index("core")
    chips = lax.axis_size("rchip")
    split = partial.reshape((chips, 2, -1) + partial.shape[1:])
    keep = jnp.where(core == 0, split[:, 0], split[:, 1])
    send = jnp.where(core == 0, split[:, 1], split[:, 0])
    arrived = lax.ppermute(send, "core", [(0, 1), (1, 0)])
    chip_sum = (keep.astype(jnp.float32) + arrived.astype(jnp.float32)).astype(jnp.bfloat16)
    pieces = lax.all_to_all(chip_sum, "rchip", 0, 0)
    return jnp.sum(pieces.astype(jnp.float32), axis=0)


def adjoint_sweep(state_grad, rate_rows, onehot, seq_count):
    channels = state_grad.shape[0]
    seq_rate = jnp.dot(onehot, rate_rows, precision=exact_mode)
    decays = (1.0 - seq_rate).T
    running = state_grad.reshape(channels, seq_count, -1)
    bins = running.shape[2]
    factor = decays[:, :, None]
    shift = 1
    while shift < bins:
        ahead = jnp.concatenate(
            [running[:, :, shift:], jnp.zeros((channels, seq_count, shift), running.dtype)], axis=2
        )
        running = running + factor * ahead
        factor = factor * factor
        shift *= 2
    return running.reshape(channels, -1)


def rate_term(adjoint, states_share, onehot, seq_count):
    channels = adjoint.shape[0]
    adjoint_seq = adjoint.reshape(channels, seq_count, -1)
    previous = states_share.astype(jnp.float32).reshape(channels, seq_count, -1)
    per_seq = jnp.sum(adjoint_seq[:, :, 1:] * previous[:, :, :-1], axis=2)
    return -jnp.dot(onehot.T, per_seq.T, precision=exact_mode)


def per_device(inputs, out_grad, states, in_weight, out_weight, decay_rate, session_ids, lengths):
    n_col = lax.axis_size("col")
    seq_count = session_ids.shape[0]
    onehot = session_table(session_ids, decay_rate.shape[0])
    grad_rows = gather_rows(out_grad, "col", n_col)
    token_total = grad_rows.shape[0]
    bin_count = token_total // seq_count
    token_ids = jnp.arange(token_total, dtype=jnp.int32)
    seq_match = (token_ids // bin_count)[:, None] == jnp.arange(seq_count, dtype=jnp.int32)[None, :]
    seq_length = jnp.sum(jnp.where(seq_match, lengths[None, :], 0), axis=1)
    valid_bin = token_ids % bin_count >= bin_count - seq_length
    masked = jnp.where(valid_bin[:, None], grad_rows, jnp.zeros_like(grad_rows))
    state_grad = scatter_channels(contract(out_weight, masked, 1, 1).astype(jnp.bfloat16))
    states_rows = gather_channels(states)
    out_weight_grad = jnp.dot(states_rows, masked, preferred_element_type=jnp.float32).astype(
        jnp.bfloat16
    )
    adjoint = adjoint_sweep(state_grad, decay_rate, onehot, seq_count)
    rate_grad = rate_term(adjoint, states, onehot, seq_count)
    gathered = gather_channels(adjoint.astype(jnp.bfloat16))
    input_rows = lax.all_gather(inputs, "col", axis=0, tiled=True)
    in_weight_grad = contract(input_rows, gathered, 0, 1).astype(jnp.bfloat16)
    input_grad = scatter_sum(
        contract(gathered, in_weight, 0, 1).astype(jnp.bfloat16), "col", n_col
    ).astype(jnp.bfloat16)
    return (input_grad, in_weight_grad, out_weight_grad, rate_grad)


def solution(mesh):
    row = ("rchip", "core")
    split_mesh = Mesh(
        mesh.devices.reshape(mesh.shape["row"] // 2, 2, mesh.shape["col"]), ("rchip", "core", "col")
    )
    return jax.shard_map(
        per_device,
        mesh=split_mesh,
        in_specs=(
            P("col", row),
            P("col", row),
            P(("col",) + row, None),
            P(row, "col"),
            P("col", row),
            P(None, ("col",) + row),
            P(),
            P(),
        ),
        out_specs=(P("col", row), P(row, "col"), P("col", row), P(None, ("col",) + row)),
        check_vma=False,
    )
```

```python
import jax
import jax.numpy as jnp
from jax import lax
from jax.sharding import Mesh, PartitionSpec as P

exact_mode = lax.Precision.HIGHEST


def contract(left_side, right_side, left_dim, right_dim):
    return lax.dot_general(
        left_side,
        right_side,
        (((left_dim,), (right_dim,)), ((), ())),
        preferred_element_type=jnp.float32,
    )


def session_table(session_ids, table_rows):
    return (session_ids[:, None] == jnp.arange(table_rows, dtype=jnp.int32)[None, :]).astype(
        jnp.float32
    )


def gather_rows(share, axis_name, parts):
    spread = jnp.broadcast_to(share[None], (parts,) + share.shape)
    return lax.all_to_all(spread, axis_name, 0, 0).reshape((-1,) + share.shape[1:])


def scatter_sum(partial, axis_name, parts):
    pieces = lax.all_to_all(partial.reshape((parts, -1) + partial.shape[1:]), axis_name, 0, 0)
    return jnp.sum(pieces.astype(jnp.float32), axis=0)


def gather_channels(share):
    core = lax.axis_index("core")
    chips = lax.axis_size("rchip")
    mine = gather_rows(share, "rchip", chips).reshape((chips, 1) + share.shape)
    other = lax.ppermute(mine, "core", [(0, 1), (1, 0)])
    ordered = jnp.where(core == 0, jnp.concatenate([mine, other], 1), jnp.concatenate([other, mine], 1))
    return ordered.reshape((-1,) + share.shape[1:])


def scatter_channels(partial, share):
    core = lax.axis_index("core")
    chips = lax.axis_size("rchip")
    split = partial.reshape((chips, 2, -1) + partial.shape[1:])
    keep = jnp.where(core == 0, split[:, 0], split[:, 1])
    send = jnp.where(core == 0, split[:, 1], split[:, 0])
    arrived = lax.ppermute(send, "core", [(0, 1), (1, 0)])
    chip_sum = (keep.astype(jnp.float32) + arrived.astype(jnp.float32)).astype(jnp.bfloat16)
    spread = jnp.broadcast_to(share[None], (chips,) + share.shape)
    pieces = lax.all_to_all(jnp.stack([chip_sum, spread], 1), "rchip", 0, 0)
    mine = pieces[:, 1].reshape((chips, 1) + share.shape)
    other = lax.ppermute(mine, "core", [(0, 1), (1, 0)])
    ordered = jnp.where(core == 0, jnp.concatenate([mine, other], 1), jnp.concatenate([other, mine], 1))
    return jnp.sum(pieces[:, 0].astype(jnp.float32), axis=0), ordered.reshape((-1,) + share.shape[1:])


def adjoint_sweep(state_grad, rate_rows, onehot, seq_count):
    channels = state_grad.shape[0]
    seq_rate = jnp.dot(onehot, rate_rows, precision=exact_mode)
    decays = (1.0 - seq_rate).T
    running = state_grad.reshape(channels, seq_count, -1)
    bins = running.shape[2]
    factor = decays[:, :, None]
    shift = 1
    while shift < bins:
        ahead = jnp.concatenate(
            [running[:, :, shift:], jnp.zeros((channels, seq_count, shift), running.dtype)], axis=2
        )
        running = running + factor * ahead
        factor = factor * factor
        shift *= 2
    return running.reshape(channels, -1)


def rate_term(adjoint, states_share, onehot, seq_count):
    channels = adjoint.shape[0]
    adjoint_seq = adjoint.reshape(channels, seq_count, -1)
    previous = states_share.astype(jnp.float32).reshape(channels, seq_count, -1)
    per_seq = jnp.sum(adjoint_seq[:, :, 1:] * previous[:, :, :-1], axis=2)
    return -jnp.dot(onehot.T, per_seq.T, precision=exact_mode)


def per_device(inputs, out_grad, states, in_weight, out_weight, decay_rate, session_ids, lengths):
    n_col = lax.axis_size("col")
    seq_count = session_ids.shape[0]
    onehot = session_table(session_ids, decay_rate.shape[0])
    grad_rows = gather_rows(out_grad, "col", n_col)
    token_total = grad_rows.shape[0]
    bin_count = token_total // seq_count
    token_ids = jnp.arange(token_total, dtype=jnp.int32)
    seq_match = (token_ids // bin_count)[:, None] == jnp.arange(seq_count, dtype=jnp.int32)[None, :]
    seq_length = jnp.sum(jnp.where(seq_match, lengths[None, :], 0), axis=1)
    valid_bin = token_ids % bin_count >= bin_count - seq_length
    masked = jnp.where(valid_bin[:, None], grad_rows, jnp.zeros_like(grad_rows))
    state_grad, states_rows = scatter_channels(
        contract(out_weight, masked, 1, 1).astype(jnp.bfloat16), states
    )
    out_weight_grad = jnp.dot(states_rows, masked, preferred_element_type=jnp.float32).astype(
        jnp.bfloat16
    )
    adjoint = adjoint_sweep(state_grad, decay_rate, onehot, seq_count)
    rate_grad = rate_term(adjoint, states, onehot, seq_count)
    gathered = gather_channels(adjoint.astype(jnp.bfloat16))
    input_columns = lax.all_gather(inputs.T, "col", axis=1, tiled=True)
    in_weight_grad = contract(input_columns, gathered, 1, 1).astype(jnp.bfloat16)
    input_grad = scatter_sum(
        contract(gathered, in_weight, 0, 1).astype(jnp.bfloat16), "col", n_col
    ).astype(jnp.bfloat16)
    return (input_grad, in_weight_grad, out_weight_grad, rate_grad)


def solution(mesh):
    row = ("rchip", "core")
    split_mesh = Mesh(
        mesh.devices.reshape(mesh.shape["row"] // 2, 2, mesh.shape["col"]), ("rchip", "core", "col")
    )
    return jax.shard_map(
        per_device,
        mesh=split_mesh,
        in_specs=(
            P("col", row),
            P("col", row),
            P(("col",) + row, None),
            P(row, "col"),
            P("col", row),
            P(None, ("col",) + row),
            P(),
            P(),
        ),
        out_specs=(P("col", row), P(row, "col"), P("col", row), P(None, ("col",) + row)),
        check_vma=False,
    )
```

```python
import jax
import jax.numpy as jnp
from jax import lax
from jax.sharding import Mesh, PartitionSpec as P

exact_mode = lax.Precision.HIGHEST


def contract(left_side, right_side, left_dim, right_dim):
    return lax.dot_general(
        left_side,
        right_side,
        (((left_dim,), (right_dim,)), ((), ())),
        preferred_element_type=jnp.float32,
    )


def session_table(session_ids, table_rows):
    return (session_ids[:, None] == jnp.arange(table_rows, dtype=jnp.int32)[None, :]).astype(
        jnp.float32
    )


def gather_rows(share, axis_name, parts):
    spread = jnp.broadcast_to(share[None], (parts,) + share.shape)
    return lax.all_to_all(spread, axis_name, 0, 0).reshape((-1,) + share.shape[1:])


def scatter_sum(partial, axis_name, parts):
    pieces = lax.all_to_all(partial.reshape((parts, -1) + partial.shape[1:]), axis_name, 0, 0)
    return jnp.sum(pieces.astype(jnp.float32), axis=0)


def gather_channels(share):
    core = lax.axis_index("core")
    chips = lax.axis_size("rchip")
    mine = gather_rows(share, "rchip", chips).reshape((chips, 1) + share.shape)
    other = lax.ppermute(mine, "core", [(0, 1), (1, 0)])
    ordered = jnp.where(core == 0, jnp.concatenate([mine, other], 1), jnp.concatenate([other, mine], 1))
    return ordered.reshape((-1,) + share.shape[1:])


def scatter_channels(partial, share):
    core = lax.axis_index("core")
    chips = lax.axis_size("rchip")
    split = partial.reshape((chips, 2, -1) + partial.shape[1:])
    keep = jnp.where(core == 0, split[:, 0], split[:, 1])
    send = jnp.where(core == 0, split[:, 1], split[:, 0])
    arrived = lax.ppermute(send, "core", [(0, 1), (1, 0)])
    chip_sum = (keep.astype(jnp.float32) + arrived.astype(jnp.float32)).astype(jnp.bfloat16)
    spread = jnp.broadcast_to(share[None], (chips,) + share.shape)
    pieces = lax.all_to_all(jnp.stack([chip_sum, spread], 1), "rchip", 0, 0)
    mine = pieces[:, 1].reshape((chips, 1) + share.shape)
    other = lax.ppermute(mine, "core", [(0, 1), (1, 0)])
    ordered = jnp.where(core == 0, jnp.concatenate([mine, other], 1), jnp.concatenate([other, mine], 1))
    return jnp.sum(pieces[:, 0].astype(jnp.float32), axis=0), ordered.reshape((-1,) + share.shape[1:])


def adjoint_sweep(state_grad, rate_rows, onehot, seq_count):
    channels = state_grad.shape[0]
    seq_rate = jnp.dot(onehot, rate_rows, precision=exact_mode)
    decays = (1.0 - seq_rate).T
    running = state_grad.reshape(channels, seq_count, -1)
    bins = running.shape[2]
    factor = decays[:, :, None]
    shift = 1
    while shift < bins:
        ahead = jnp.concatenate(
            [running[:, :, shift:], jnp.zeros((channels, seq_count, shift), running.dtype)], axis=2
        )
        running = running + factor * ahead
        factor = factor * factor
        shift *= 2
    return running.reshape(channels, -1)


def rate_term(adjoint, states_share, onehot, seq_count):
    channels = adjoint.shape[0]
    adjoint_seq = adjoint.reshape(channels, seq_count, -1)
    previous = states_share.astype(jnp.float32).reshape(channels, seq_count, -1)
    per_seq = jnp.sum(adjoint_seq[:, :, 1:] * previous[:, :, :-1], axis=2)
    return -jnp.dot(onehot.T, per_seq.T, precision=exact_mode)


def per_device(inputs, out_grad, states, in_weight, out_weight, decay_rate, session_ids, lengths):
    n_col = lax.axis_size("col")
    seq_count = session_ids.shape[0]
    onehot = session_table(session_ids, decay_rate.shape[0])
    grad_rows = gather_rows(out_grad, "col", n_col)
    token_total = grad_rows.shape[0]
    bin_count = token_total // seq_count
    token_ids = jnp.arange(token_total, dtype=jnp.int32)
    seq_match = (token_ids // bin_count)[:, None] == jnp.arange(seq_count, dtype=jnp.int32)[None, :]
    seq_length = jnp.sum(jnp.where(seq_match, lengths[None, :], 0), axis=1)
    valid_bin = token_ids % bin_count >= bin_count - seq_length
    masked = jnp.where(valid_bin[:, None], grad_rows, jnp.zeros_like(grad_rows))
    state_grad, states_rows = scatter_channels(
        contract(out_weight, masked, 1, 1).astype(jnp.bfloat16), states
    )
    out_weight_grad = jnp.dot(states_rows, masked, preferred_element_type=jnp.float32).astype(
        jnp.bfloat16
    )
    adjoint = adjoint_sweep(state_grad, decay_rate, onehot, seq_count)
    rate_grad = rate_term(adjoint, states, onehot, seq_count)
    gathered = gather_channels(adjoint.astype(jnp.bfloat16))
    input_columns = lax.all_gather(inputs.T, "col", axis=1, tiled=True)
    in_weight_grad = contract(input_columns, gathered, 1, 1).astype(jnp.bfloat16)
    partial = contract(gathered, in_weight, 0, 1).astype(jnp.bfloat16)
    pieces = lax.all_to_all(partial.reshape((n_col, -1) + partial.shape[1:]), "col", 0, 0)
    pieces, in_weight_grad = lax.optimization_barrier((pieces, in_weight_grad))
    input_grad = jnp.sum(pieces.astype(jnp.float32), axis=0).astype(jnp.bfloat16)
    return (input_grad, in_weight_grad, out_weight_grad, rate_grad)


def solution(mesh):
    row = ("rchip", "core")
    split_mesh = Mesh(
        mesh.devices.reshape(mesh.shape["row"] // 2, 2, mesh.shape["col"]), ("rchip", "core", "col")
    )
    return jax.shard_map(
        per_device,
        mesh=split_mesh,
        in_specs=(
            P("col", row),
            P("col", row),
            P(("col",) + row, None),
            P(row, "col"),
            P("col", row),
            P(None, ("col",) + row),
            P(),
            P(),
        ),
        out_specs=(P("col", row), P(row, "col"), P("col", row), P(None, ("col",) + row)),
        check_vma=False,
    )
```

```python
import jax
import jax.numpy as jnp
from jax import lax
from jax.sharding import Mesh, PartitionSpec as P

exact_mode = lax.Precision.HIGHEST


def contract(left_side, right_side, left_dim, right_dim):
    return lax.dot_general(
        left_side,
        right_side,
        (((left_dim,), (right_dim,)), ((), ())),
        preferred_element_type=jnp.float32,
    )


def session_table(session_ids, table_rows):
    return (session_ids[:, None] == jnp.arange(table_rows, dtype=jnp.int32)[None, :]).astype(
        jnp.float32
    )


def gather_rows(share, axis_name, parts):
    spread = jnp.broadcast_to(share[None], (parts,) + share.shape)
    return lax.all_to_all(spread, axis_name, 0, 0).reshape((-1,) + share.shape[1:])


def scatter_sum(partial, axis_name, parts):
    pieces = lax.all_to_all(partial.reshape((parts, -1) + partial.shape[1:]), axis_name, 0, 0)
    return jnp.sum(pieces.astype(jnp.float32), axis=0)


def gather_channels(share):
    core = lax.axis_index("core")
    chips = lax.axis_size("rchip")
    mine = gather_rows(share, "rchip", chips).reshape((chips, 1) + share.shape)
    other = lax.ppermute(mine, "core", [(0, 1), (1, 0)])
    ordered = jnp.where(core == 0, jnp.concatenate([mine, other], 1), jnp.concatenate([other, mine], 1))
    return ordered.reshape((-1,) + share.shape[1:])


def scatter_channels(partial, share):
    core = lax.axis_index("core")
    chips = lax.axis_size("rchip")
    split = partial.reshape((chips, 2, -1) + partial.shape[1:])
    keep = jnp.where(core == 0, split[:, 0], split[:, 1])
    send = jnp.where(core == 0, split[:, 1], split[:, 0])
    arrived = lax.ppermute(send, "core", [(0, 1), (1, 0)])
    chip_sum = (keep.astype(jnp.float32) + arrived.astype(jnp.float32)).astype(jnp.bfloat16)
    spread = jnp.broadcast_to(share[None], (chips,) + share.shape)
    pieces = lax.all_to_all(jnp.stack([chip_sum, spread], 1), "rchip", 0, 0)
    mine = pieces[:, 1].reshape((chips, 1) + share.shape)
    other = lax.ppermute(mine, "core", [(0, 1), (1, 0)])
    ordered = jnp.where(core == 0, jnp.concatenate([mine, other], 1), jnp.concatenate([other, mine], 1))
    return jnp.sum(pieces[:, 0].astype(jnp.float32), axis=0), ordered.reshape((-1,) + share.shape[1:])


def adjoint_sweep(state_grad, rate_rows, onehot, seq_count):
    channels = state_grad.shape[0]
    seq_rate = jnp.dot(onehot, rate_rows, precision=exact_mode)
    decays = (1.0 - seq_rate).T
    running = state_grad.reshape(channels, seq_count, -1)
    bins = running.shape[2]
    factor = decays[:, :, None]
    shift = 1
    while shift < bins:
        ahead = jnp.concatenate(
            [running[:, :, shift:], jnp.zeros((channels, seq_count, shift), running.dtype)], axis=2
        )
        running = running + factor * ahead
        factor = factor * factor
        shift *= 2
    return running.reshape(channels, -1)


def rate_term(adjoint, states_share, onehot, seq_count):
    channels = adjoint.shape[0]
    adjoint_seq = adjoint.reshape(channels, seq_count, -1)
    previous = states_share.astype(jnp.float32).reshape(channels, seq_count, -1)
    per_seq = jnp.sum(adjoint_seq[:, :, 1:] * previous[:, :, :-1], axis=2)
    return -jnp.dot(onehot.T, per_seq.T, precision=exact_mode)


def per_device(inputs, out_grad, states, in_weight, out_weight, decay_rate, session_ids, lengths):
    n_col = lax.axis_size("col")
    seq_count = session_ids.shape[0]
    onehot = session_table(session_ids, decay_rate.shape[0])
    grad_rows = gather_rows(out_grad, "col", n_col)
    token_total = grad_rows.shape[0]
    bin_count = token_total // seq_count
    token_ids = jnp.arange(token_total, dtype=jnp.int32)
    seq_match = (token_ids // bin_count)[:, None] == jnp.arange(seq_count, dtype=jnp.int32)[None, :]
    seq_length = jnp.sum(jnp.where(seq_match, lengths[None, :], 0), axis=1)
    valid_bin = token_ids % bin_count >= bin_count - seq_length
    masked = jnp.where(valid_bin[:, None], grad_rows, jnp.zeros_like(grad_rows))
    state_grad, states_rows = scatter_channels(
        contract(out_weight, masked, 1, 1).astype(jnp.bfloat16), states
    )
    out_weight_grad = jnp.dot(states_rows, masked, preferred_element_type=jnp.float32).astype(
        jnp.bfloat16
    )
    adjoint = adjoint_sweep(state_grad, decay_rate, onehot, seq_count)
    rate_grad = rate_term(adjoint, states, onehot, seq_count)
    gathered = gather_channels(adjoint.astype(jnp.bfloat16))
    inputs_late, _ = lax.optimization_barrier((inputs, masked))
    input_columns = lax.all_gather(inputs_late.T, "col", axis=1, tiled=True)
    in_weight_grad = contract(input_columns, gathered, 1, 1).astype(jnp.bfloat16)
    partial = contract(gathered, in_weight, 0, 1).astype(jnp.bfloat16)
    pieces = lax.all_to_all(partial.reshape((n_col, -1) + partial.shape[1:]), "col", 0, 0)
    pieces, in_weight_grad = lax.optimization_barrier((pieces, in_weight_grad))
    input_grad = jnp.sum(pieces.astype(jnp.float32), axis=0).astype(jnp.bfloat16)
    return (input_grad, in_weight_grad, out_weight_grad, rate_grad)


def solution(mesh):
    row = ("rchip", "core")
    split_mesh = Mesh(
        mesh.devices.reshape(mesh.shape["row"] // 2, 2, mesh.shape["col"]), ("rchip", "core", "col")
    )
    return jax.shard_map(
        per_device,
        mesh=split_mesh,
        in_specs=(
            P("col", row),
            P("col", row),
            P(("col",) + row, None),
            P(row, "col"),
            P("col", row),
            P(None, ("col",) + row),
            P(),
            P(),
        ),
        out_specs=(P("col", row), P(row, "col"), P("col", row), P(None, ("col",) + row)),
        check_vma=False,
    )
```

```python
import jax
import jax.numpy as jnp
from jax import lax
from jax.sharding import Mesh, PartitionSpec as P

exact_mode = lax.Precision.HIGHEST


def contract(left_side, right_side, left_dim, right_dim):
    return lax.dot_general(
        left_side,
        right_side,
        (((left_dim,), (right_dim,)), ((), ())),
        preferred_element_type=jnp.float32,
    )


def session_table(session_ids, table_rows):
    return (session_ids[:, None] == jnp.arange(table_rows, dtype=jnp.int32)[None, :]).astype(
        jnp.float32
    )


def gather_rows(share, axis_name, parts):
    spread = jnp.broadcast_to(share[None], (parts,) + share.shape)
    return lax.all_to_all(spread, axis_name, 0, 0).reshape((-1,) + share.shape[1:])


def scatter_sum(partial, axis_name, parts):
    pieces = lax.all_to_all(partial.reshape((parts, -1) + partial.shape[1:]), axis_name, 0, 0)
    return jnp.sum(pieces.astype(jnp.float32), axis=0)


def gather_channels(share):
    core = lax.axis_index("core")
    chips = lax.axis_size("rchip")
    mine = gather_rows(share, "rchip", chips).reshape((chips, 1) + share.shape)
    other = lax.ppermute(mine, "core", [(0, 1), (1, 0)])
    ordered = jnp.where(core == 0, jnp.concatenate([mine, other], 1), jnp.concatenate([other, mine], 1))
    return ordered.reshape((-1,) + share.shape[1:])


def scatter_channels(partial):
    core = lax.axis_index("core")
    chips = lax.axis_size("rchip")
    split = partial.reshape((chips, 2, -1) + partial.shape[1:])
    keep = jnp.where(core == 0, split[:, 0], split[:, 1])
    send = jnp.where(core == 0, split[:, 1], split[:, 0])
    arrived = lax.ppermute(send, "core", [(0, 1), (1, 0)])
    chip_sum = (keep.astype(jnp.float32) + arrived.astype(jnp.float32)).astype(jnp.bfloat16)
    pieces = lax.all_to_all(chip_sum, "rchip", 0, 0)
    return jnp.sum(pieces.astype(jnp.float32), axis=0)


def adjoint_sweep(state_grad, rate_rows, onehot, seq_count):
    channels = state_grad.shape[0]
    seq_rate = jnp.dot(onehot, rate_rows, precision=exact_mode)
    decays = (1.0 - seq_rate).T
    running = state_grad.reshape(channels, seq_count, -1)
    bins = running.shape[2]
    factor = decays[:, :, None]
    shift = 1
    while shift < bins:
        ahead = jnp.concatenate(
            [running[:, :, shift:], jnp.zeros((channels, seq_count, shift), running.dtype)], axis=2
        )
        running = running + factor * ahead
        factor = factor * factor
        shift *= 2
    return running.reshape(channels, -1)


def rate_term(adjoint, states_share, onehot, seq_count):
    channels = adjoint.shape[0]
    adjoint_seq = adjoint.reshape(channels, seq_count, -1)
    previous = states_share.astype(jnp.float32).reshape(channels, seq_count, -1)
    per_seq = jnp.sum(adjoint_seq[:, :, 1:] * previous[:, :, :-1], axis=2)
    return -jnp.dot(onehot.T, per_seq.T, precision=exact_mode)


def per_device(inputs, out_grad, states, in_weight, out_weight, decay_rate, session_ids, lengths):
    n_col = lax.axis_size("col")
    seq_count = session_ids.shape[0]
    onehot = session_table(session_ids, decay_rate.shape[0])
    grad_rows = gather_rows(out_grad, "col", n_col)
    token_total = grad_rows.shape[0]
    bin_count = token_total // seq_count
    token_ids = jnp.arange(token_total, dtype=jnp.int32)
    seq_match = (token_ids // bin_count)[:, None] == jnp.arange(seq_count, dtype=jnp.int32)[None, :]
    seq_length = jnp.sum(jnp.where(seq_match, lengths[None, :], 0), axis=1)
    valid_bin = token_ids % bin_count >= bin_count - seq_length
    masked = jnp.where(valid_bin[:, None], grad_rows, jnp.zeros_like(grad_rows))
    state_grad = scatter_channels(contract(out_weight, masked, 1, 1).astype(jnp.bfloat16))
    states_rows = lax.all_gather(states, ("rchip", "core"), axis=0, tiled=True)
    out_weight_grad = jnp.dot(states_rows, masked, preferred_element_type=jnp.float32).astype(
        jnp.bfloat16
    )
    adjoint = adjoint_sweep(state_grad, decay_rate, onehot, seq_count)
    rate_grad = rate_term(adjoint, states, onehot, seq_count)
    gathered = gather_channels(adjoint.astype(jnp.bfloat16))
    inputs_late, _ = lax.optimization_barrier((inputs, masked))
    input_columns = lax.all_gather(inputs_late.T, "col", axis=1, tiled=True)
    in_weight_grad = contract(input_columns, gathered, 1, 1).astype(jnp.bfloat16)
    partial = contract(gathered, in_weight, 0, 1).astype(jnp.bfloat16)
    pieces = lax.all_to_all(partial.reshape((n_col, -1) + partial.shape[1:]), "col", 0, 0)
    pieces, in_weight_grad, out_weight_grad = lax.optimization_barrier(
        (pieces, in_weight_grad, out_weight_grad)
    )
    input_grad = jnp.sum(pieces.astype(jnp.float32), axis=0).astype(jnp.bfloat16)
    return (input_grad, in_weight_grad, out_weight_grad, rate_grad)


def solution(mesh):
    row = ("rchip", "core")
    split_mesh = Mesh(
        mesh.devices.reshape(mesh.shape["row"] // 2, 2, mesh.shape["col"]), ("rchip", "core", "col")
    )
    return jax.shard_map(
        per_device,
        mesh=split_mesh,
        in_specs=(
            P("col", row),
            P("col", row),
            P(("col",) + row, None),
            P(row, "col"),
            P("col", row),
            P(None, ("col",) + row),
            P(),
            P(),
        ),
        out_specs=(P("col", row), P(row, "col"), P("col", row), P(None, ("col",) + row)),
        check_vma=False,
    )
```

```python
import jax
import jax.numpy as jnp
from jax import lax
from jax.sharding import Mesh, PartitionSpec as P

exact_mode = lax.Precision.HIGHEST


def contract(left_side, right_side, left_dim, right_dim):
    return lax.dot_general(
        left_side,
        right_side,
        (((left_dim,), (right_dim,)), ((), ())),
        preferred_element_type=jnp.float32,
    )


def session_table(session_ids, table_rows):
    return (session_ids[:, None] == jnp.arange(table_rows, dtype=jnp.int32)[None, :]).astype(
        jnp.float32
    )


def gather_rows(share, axis_name, parts):
    spread = jnp.broadcast_to(share[None], (parts,) + share.shape)
    return lax.all_to_all(spread, axis_name, 0, 0).reshape((-1,) + share.shape[1:])


def scatter_sum(partial, axis_name, parts):
    pieces = lax.all_to_all(partial.reshape((parts, -1) + partial.shape[1:]), axis_name, 0, 0)
    return jnp.sum(pieces.astype(jnp.float32), axis=0)


def swap_cores(mine):
    core = lax.axis_index("core")
    chips = lax.axis_size("rchip")
    mine = mine.reshape((chips, 1, -1) + mine.shape[1:])
    other = lax.ppermute(mine, "core", [(0, 1), (1, 0)])
    ordered = jnp.where(core == 0, jnp.concatenate([mine, other], 1), jnp.concatenate([other, mine], 1))
    return ordered.reshape((-1,) + mine.shape[3:])


def gather_channels(share):
    core = lax.axis_index("core")
    chips = lax.axis_size("rchip")
    mine = gather_rows(share, "rchip", chips).reshape((chips, 1) + share.shape)
    other = lax.ppermute(mine, "core", [(0, 1), (1, 0)])
    ordered = jnp.where(core == 0, jnp.concatenate([mine, other], 1), jnp.concatenate([other, mine], 1))
    return ordered.reshape((-1,) + share.shape[1:])


def scatter_channels(partial):
    core = lax.axis_index("core")
    chips = lax.axis_size("rchip")
    split = partial.reshape((chips, 2, -1) + partial.shape[1:])
    keep = jnp.where(core == 0, split[:, 0], split[:, 1])
    send = jnp.where(core == 0, split[:, 1], split[:, 0])
    arrived = lax.ppermute(send, "core", [(0, 1), (1, 0)])
    chip_sum = (keep.astype(jnp.float32) + arrived.astype(jnp.float32)).astype(jnp.bfloat16)
    pieces = lax.all_to_all(chip_sum, "rchip", 0, 0)
    return jnp.sum(pieces.astype(jnp.float32), axis=0)


def adjoint_sweep(state_grad, rate_rows, onehot, seq_count):
    channels = state_grad.shape[0]
    seq_rate = jnp.dot(onehot, rate_rows, precision=exact_mode)
    decays = (1.0 - seq_rate).T
    running = state_grad.reshape(channels, seq_count, -1)
    bins = running.shape[2]
    factor = decays[:, :, None]
    shift = 1
    while shift < bins:
        ahead = jnp.concatenate(
            [running[:, :, shift:], jnp.zeros((channels, seq_count, shift), running.dtype)], axis=2
        )
        running = running + factor * ahead
        factor = factor * factor
        shift *= 2
    return running.reshape(channels, -1)


def rate_term(adjoint, states_share, onehot, seq_count):
    channels = adjoint.shape[0]
    adjoint_seq = adjoint.reshape(channels, seq_count, -1)
    previous = states_share.astype(jnp.float32).reshape(channels, seq_count, -1)
    per_seq = jnp.sum(adjoint_seq[:, :, 1:] * previous[:, :, :-1], axis=2)
    return -jnp.dot(onehot.T, per_seq.T, precision=exact_mode)


def per_device(inputs, out_grad, states, in_weight, out_weight, decay_rate, session_ids, lengths):
    n_col = lax.axis_size("col")
    seq_count = session_ids.shape[0]
    onehot = session_table(session_ids, decay_rate.shape[0])
    grad_rows = gather_rows(out_grad, "col", n_col)
    token_total = grad_rows.shape[0]
    bin_count = token_total // seq_count
    token_ids = jnp.arange(token_total, dtype=jnp.int32)
    seq_match = (token_ids // bin_count)[:, None] == jnp.arange(seq_count, dtype=jnp.int32)[None, :]
    seq_length = jnp.sum(jnp.where(seq_match, lengths[None, :], 0), axis=1)
    valid_bin = token_ids % bin_count >= bin_count - seq_length
    masked = jnp.where(valid_bin[:, None], grad_rows, jnp.zeros_like(grad_rows))
    state_grad = scatter_channels(contract(out_weight, masked, 1, 1).astype(jnp.bfloat16))
    states_rows = swap_cores(lax.all_gather(states, "rchip", axis=0, tiled=True))
    masked_columns = jnp.where(valid_bin[None, :], grad_rows.T, jnp.zeros_like(grad_rows.T))
    out_weight_grad = contract(states_rows, masked_columns, 1, 1).astype(jnp.bfloat16)
    adjoint = adjoint_sweep(state_grad, decay_rate, onehot, seq_count)
    rate_grad = rate_term(adjoint, states, onehot, seq_count)
    gathered = gather_channels(adjoint.astype(jnp.bfloat16))
    inputs_held, _ = lax.optimization_barrier((inputs, out_grad))
    input_columns = lax.all_gather(inputs_held.T, "col", axis=1, tiled=True)
    in_weight_grad = contract(input_columns, gathered, 1, 1).astype(jnp.bfloat16)
    partial = contract(gathered, in_weight, 0, 1).astype(jnp.bfloat16)
    pieces = lax.all_to_all(partial.reshape((n_col, -1) + partial.shape[1:]), "col", 0, 0)
    pieces, in_weight_grad, out_weight_grad = lax.optimization_barrier(
        (pieces, in_weight_grad, out_weight_grad)
    )
    input_grad = jnp.sum(pieces.astype(jnp.float32), axis=0).astype(jnp.bfloat16)
    return (input_grad, in_weight_grad, out_weight_grad, rate_grad)


def solution(mesh):
    row = ("rchip", "core")
    split_mesh = Mesh(
        mesh.devices.reshape(mesh.shape["row"] // 2, 2, mesh.shape["col"]), ("rchip", "core", "col")
    )
    return jax.shard_map(
        per_device,
        mesh=split_mesh,
        in_specs=(
            P("col", row),
            P("col", row),
            P(("col",) + row, None),
            P(row, "col"),
            P("col", row),
            P(None, ("col",) + row),
            P(),
            P(),
        ),
        out_specs=(P("col", row), P(row, "col"), P("col", row), P(None, ("col",) + row)),
        check_vma=False,
    )
```

```python
import jax
import jax.numpy as jnp
from jax import lax
from jax.sharding import Mesh, PartitionSpec as P

exact_mode = lax.Precision.HIGHEST


def contract(left_side, right_side, left_dim, right_dim):
    return lax.dot_general(
        left_side,
        right_side,
        (((left_dim,), (right_dim,)), ((), ())),
        preferred_element_type=jnp.float32,
    )


def session_table(session_ids, table_rows):
    return (session_ids[:, None] == jnp.arange(table_rows, dtype=jnp.int32)[None, :]).astype(
        jnp.float32
    )


def gather_rows(share, axis_name, parts):
    spread = jnp.broadcast_to(share[None], (parts,) + share.shape)
    return lax.all_to_all(spread, axis_name, 0, 0).reshape((-1,) + share.shape[1:])


def scatter_sum(partial, axis_name, parts):
    pieces = lax.all_to_all(partial.reshape((parts, -1) + partial.shape[1:]), axis_name, 0, 0)
    return jnp.sum(pieces.astype(jnp.float32), axis=0)


def swap_cores(mine):
    core = lax.axis_index("core")
    chips = lax.axis_size("rchip")
    mine = mine.reshape((chips, 1, -1) + mine.shape[1:])
    other = lax.ppermute(mine, "core", [(0, 1), (1, 0)])
    ordered = jnp.where(core == 0, jnp.concatenate([mine, other], 1), jnp.concatenate([other, mine], 1))
    return ordered.reshape((-1,) + mine.shape[3:])


def gather_channels(share):
    core = lax.axis_index("core")
    chips = lax.axis_size("rchip")
    mine = gather_rows(share, "rchip", chips).reshape((chips, 1) + share.shape)
    other = lax.ppermute(mine, "core", [(0, 1), (1, 0)])
    ordered = jnp.where(core == 0, jnp.concatenate([mine, other], 1), jnp.concatenate([other, mine], 1))
    return ordered.reshape((-1,) + share.shape[1:])


def scatter_channels(partial):
    core = lax.axis_index("core")
    chips = lax.axis_size("rchip")
    split = partial.reshape((chips, 2, -1) + partial.shape[1:])
    keep = jnp.where(core == 0, split[:, 0], split[:, 1])
    send = jnp.where(core == 0, split[:, 1], split[:, 0])
    arrived = lax.ppermute(send, "core", [(0, 1), (1, 0)])
    chip_sum = (keep.astype(jnp.float32) + arrived.astype(jnp.float32)).astype(jnp.bfloat16)
    pieces = lax.all_to_all(chip_sum, "rchip", 0, 0)
    return jnp.sum(pieces.astype(jnp.float32), axis=0)


def adjoint_sweep(state_grad, rate_rows, onehot, seq_count):
    channels = state_grad.shape[0]
    seq_rate = jnp.dot(onehot, rate_rows, precision=exact_mode)
    decays = (1.0 - seq_rate).T
    running = state_grad.reshape(channels, seq_count, -1)
    bins = running.shape[2]
    factor = decays[:, :, None]
    shift = 1
    while shift < bins:
        ahead = jnp.concatenate(
            [running[:, :, shift:], jnp.zeros((channels, seq_count, shift), running.dtype)], axis=2
        )
        running = running + factor * ahead
        factor = factor * factor
        shift *= 2
    return running.reshape(channels, -1)


def rate_term(adjoint, states_share, onehot, seq_count):
    channels = adjoint.shape[0]
    adjoint_seq = adjoint.reshape(channels, seq_count, -1)
    previous = states_share.astype(jnp.float32).reshape(channels, seq_count, -1)
    per_seq = jnp.sum(adjoint_seq[:, :, 1:] * previous[:, :, :-1], axis=2)
    return -jnp.dot(onehot.T, per_seq.T, precision=exact_mode)


def per_device(inputs, out_grad, states, in_weight, out_weight, decay_rate, session_ids, lengths):
    n_col = lax.axis_size("col")
    seq_count = session_ids.shape[0]
    onehot = session_table(session_ids, decay_rate.shape[0])
    share = out_grad.shape[0]
    token_total = share * n_col
    bin_count = token_total // seq_count
    token_ids = lax.axis_index("col") * share + jnp.arange(share, dtype=jnp.int32)
    seq_match = (token_ids // bin_count)[:, None] == jnp.arange(seq_count, dtype=jnp.int32)[None, :]
    seq_length = jnp.sum(jnp.where(seq_match, lengths[None, :], 0), axis=1)
    valid_bin = token_ids % bin_count >= bin_count - seq_length
    masked = gather_rows(jnp.where(valid_bin[:, None], out_grad, jnp.zeros_like(out_grad)), "col", n_col)
    state_grad = scatter_channels(contract(out_weight, masked, 1, 1).astype(jnp.bfloat16))
    states_rows = swap_cores(lax.all_gather(states, "rchip", axis=0, tiled=True))
    out_weight_grad = contract(states_rows, masked.T, 1, 1).astype(jnp.bfloat16)
    adjoint = adjoint_sweep(state_grad, decay_rate, onehot, seq_count)
    rate_grad = rate_term(adjoint, states, onehot, seq_count)
    gathered = gather_channels(adjoint.astype(jnp.bfloat16))
    inputs_held, _ = lax.optimization_barrier((inputs, out_grad))
    input_columns = lax.all_gather(inputs_held.T, "col", axis=1, tiled=True)
    in_weight_grad = contract(input_columns, gathered, 1, 1).astype(jnp.bfloat16)
    partial = contract(gathered, in_weight, 0, 1).astype(jnp.bfloat16)
    pieces = lax.all_to_all(partial.reshape((n_col, -1) + partial.shape[1:]), "col", 0, 0)
    pieces, in_weight_grad, out_weight_grad = lax.optimization_barrier(
        (pieces, in_weight_grad, out_weight_grad)
    )
    input_grad = jnp.sum(pieces.astype(jnp.float32), axis=0).astype(jnp.bfloat16)
    return (input_grad, in_weight_grad, out_weight_grad, rate_grad)


def solution(mesh):
    row = ("rchip", "core")
    split_mesh = Mesh(
        mesh.devices.reshape(mesh.shape["row"] // 2, 2, mesh.shape["col"]), ("rchip", "core", "col")
    )
    return jax.shard_map(
        per_device,
        mesh=split_mesh,
        in_specs=(
            P("col", row),
            P("col", row),
            P(("col",) + row, None),
            P(row, "col"),
            P("col", row),
            P(None, ("col",) + row),
            P(),
            P(),
        ),
        out_specs=(P("col", row), P(row, "col"), P("col", row), P(None, ("col",) + row)),
        check_vma=False,
    )
```

```python
import jax
import jax.numpy as jnp
from jax import lax
from jax.sharding import Mesh, PartitionSpec as P

exact_mode = lax.Precision.HIGHEST


def contract(left_side, right_side, left_dim, right_dim):
    return lax.dot_general(
        left_side,
        right_side,
        (((left_dim,), (right_dim,)), ((), ())),
        preferred_element_type=jnp.float32,
    )


def session_table(session_ids, table_rows):
    return (session_ids[:, None] == jnp.arange(table_rows, dtype=jnp.int32)[None, :]).astype(
        jnp.float32
    )


def gather_rows(share, axis_name, parts):
    spread = jnp.broadcast_to(share[None], (parts,) + share.shape)
    return lax.all_to_all(spread, axis_name, 0, 0).reshape((-1,) + share.shape[1:])


def scatter_sum(partial, axis_name, parts):
    pieces = lax.all_to_all(partial.reshape((parts, -1) + partial.shape[1:]), axis_name, 0, 0)
    return jnp.sum(pieces.astype(jnp.float32), axis=0)


def swap_cores(mine):
    core = lax.axis_index("core")
    chips = lax.axis_size("rchip")
    mine = mine.reshape((chips, 1, -1) + mine.shape[1:])
    other = lax.ppermute(mine, "core", [(0, 1), (1, 0)])
    ordered = jnp.where(core == 0, jnp.concatenate([mine, other], 1), jnp.concatenate([other, mine], 1))
    return ordered.reshape((-1,) + mine.shape[3:])


def gather_channels(share):
    core = lax.axis_index("core")
    chips = lax.axis_size("rchip")
    mine = gather_rows(share, "rchip", chips).reshape((chips, 1) + share.shape)
    other = lax.ppermute(mine, "core", [(0, 1), (1, 0)])
    ordered = jnp.where(core == 0, jnp.concatenate([mine, other], 1), jnp.concatenate([other, mine], 1))
    return ordered.reshape((-1,) + share.shape[1:])


def scatter_channels(partial):
    core = lax.axis_index("core")
    chips = lax.axis_size("rchip")
    split = partial.reshape((chips, 2, -1) + partial.shape[1:])
    keep = jnp.where(core == 0, split[:, 0], split[:, 1])
    send = jnp.where(core == 0, split[:, 1], split[:, 0])
    arrived = lax.ppermute(send, "core", [(0, 1), (1, 0)])
    chip_sum = (keep.astype(jnp.float32) + arrived.astype(jnp.float32)).astype(jnp.bfloat16)
    pieces = lax.all_to_all(chip_sum, "rchip", 0, 0)
    return jnp.sum(pieces.astype(jnp.float32), axis=0)


def adjoint_sweep(state_grad, rate_rows, onehot, seq_count):
    channels = state_grad.shape[0]
    seq_rate = jnp.dot(onehot, rate_rows, precision=exact_mode)
    decays = (1.0 - seq_rate).T
    running = state_grad.reshape(channels, seq_count, -1)
    bins = running.shape[2]
    factor = decays[:, :, None]
    shift = 1
    while shift < bins:
        ahead = jnp.concatenate(
            [running[:, :, shift:], jnp.zeros((channels, seq_count, shift), running.dtype)], axis=2
        )
        running = running + factor * ahead
        factor = factor * factor
        shift *= 2
    return running.reshape(channels, -1)


def rate_term(adjoint, states_share, onehot, seq_count):
    channels = adjoint.shape[0]
    adjoint_seq = adjoint.reshape(channels, seq_count, -1)
    previous = states_share.astype(jnp.float32).reshape(channels, seq_count, -1)
    per_seq = jnp.sum(adjoint_seq[:, :, 1:] * previous[:, :, :-1], axis=2)
    return -jnp.dot(onehot.T, per_seq.T, precision=exact_mode)


def per_device(inputs, out_grad, states, in_weight, out_weight, decay_rate, session_ids, lengths):
    n_col = lax.axis_size("col")
    seq_count = session_ids.shape[0]
    onehot = session_table(session_ids, decay_rate.shape[0])
    grad_rows = gather_rows(out_grad, "col", n_col)
    token_total = grad_rows.shape[0]
    bin_count = token_total // seq_count
    token_ids = jnp.arange(token_total, dtype=jnp.int32)
    seq_match = (token_ids // bin_count)[:, None] == jnp.arange(seq_count, dtype=jnp.int32)[None, :]
    seq_length = jnp.sum(jnp.where(seq_match, lengths[None, :], 0), axis=1)
    valid_bin = token_ids % bin_count >= bin_count - seq_length
    masked = jnp.where(valid_bin[:, None], grad_rows, jnp.zeros_like(grad_rows))
    state_grad = scatter_channels(contract(out_weight, masked, 1, 1).astype(jnp.bfloat16))
    states_rows = swap_cores(lax.all_gather(states, "rchip", axis=0, tiled=True))
    masked_columns = jnp.where(valid_bin[None, :], grad_rows.T, jnp.zeros_like(grad_rows.T))
    out_weight_grad = contract(states_rows, masked_columns, 1, 1).astype(jnp.bfloat16)
    adjoint = adjoint_sweep(state_grad, decay_rate, onehot, seq_count)
    rate_grad = rate_term(adjoint, states, onehot, seq_count)
    gathered = gather_channels(adjoint.astype(jnp.bfloat16))
    inputs_held, _ = lax.optimization_barrier((inputs, out_grad))
    input_columns = lax.all_gather(inputs_held.T, "col", axis=1, tiled=True)
    in_weight_grad = contract(input_columns, gathered, 1, 1).astype(jnp.bfloat16)
    half = in_weight.shape[0] // 2
    sent = []
    for part in (in_weight[:half], in_weight[half:]):
        partial = contract(gathered, part, 0, 1).astype(jnp.bfloat16)
        sent.append(lax.all_to_all(partial.reshape((n_col, -1) + partial.shape[1:]), "col", 0, 0))
    first = jnp.sum(sent[0].astype(jnp.float32), axis=0)
    first, second, in_weight_grad, out_weight_grad = lax.optimization_barrier(
        (first, sent[1], in_weight_grad, out_weight_grad)
    )
    input_grad = jnp.concatenate(
        [first, jnp.sum(second.astype(jnp.float32), axis=0)], axis=1
    ).astype(jnp.bfloat16)
    return (input_grad, in_weight_grad, out_weight_grad, rate_grad)


def solution(mesh):
    row = ("rchip", "core")
    split_mesh = Mesh(
        mesh.devices.reshape(mesh.shape["row"] // 2, 2, mesh.shape["col"]), ("rchip", "core", "col")
    )
    return jax.shard_map(
        per_device,
        mesh=split_mesh,
        in_specs=(
            P("col", row),
            P("col", row),
            P(("col",) + row, None),
            P(row, "col"),
            P("col", row),
            P(None, ("col",) + row),
            P(),
            P(),
        ),
        out_specs=(P("col", row), P(row, "col"), P("col", row), P(None, ("col",) + row)),
        check_vma=False,
    )
```

```python
import jax
import jax.numpy as jnp
from jax import lax
from jax.sharding import Mesh, PartitionSpec as P

exact_mode = lax.Precision.HIGHEST


def contract(left_side, right_side, left_dim, right_dim):
    return lax.dot_general(
        left_side,
        right_side,
        (((left_dim,), (right_dim,)), ((), ())),
        preferred_element_type=jnp.float32,
    )


def session_table(session_ids, table_rows):
    return (session_ids[:, None] == jnp.arange(table_rows, dtype=jnp.int32)[None, :]).astype(
        jnp.float32
    )


def gather_rows(share, axis_name, parts):
    spread = jnp.broadcast_to(share[None], (parts,) + share.shape)
    return lax.all_to_all(spread, axis_name, 0, 0).reshape((-1,) + share.shape[1:])


def scatter_sum(partial, axis_name, parts):
    pieces = lax.all_to_all(partial.reshape((parts, -1) + partial.shape[1:]), axis_name, 0, 0)
    return jnp.sum(pieces.astype(jnp.float32), axis=0)


def swap_cores(mine):
    core = lax.axis_index("core")
    chips = lax.axis_size("rchip")
    mine = mine.reshape((chips, 1, -1) + mine.shape[1:])
    other = lax.ppermute(mine, "core", [(0, 1), (1, 0)])
    ordered = jnp.where(core == 0, jnp.concatenate([mine, other], 1), jnp.concatenate([other, mine], 1))
    return ordered.reshape((-1,) + mine.shape[3:])


def gather_channels(share):
    core = lax.axis_index("core")
    chips = lax.axis_size("rchip")
    mine = gather_rows(share, "rchip", chips).reshape((chips, 1) + share.shape)
    other = lax.ppermute(mine, "core", [(0, 1), (1, 0)])
    ordered = jnp.where(core == 0, jnp.concatenate([mine, other], 1), jnp.concatenate([other, mine], 1))
    flat = (-1,) + share.shape[1:]
    return ordered.reshape(flat), mine.reshape(flat), other.reshape(flat)


def scatter_channels(partial):
    core = lax.axis_index("core")
    chips = lax.axis_size("rchip")
    split = partial.reshape((chips, 2, -1) + partial.shape[1:])
    keep = jnp.where(core == 0, split[:, 0], split[:, 1])
    send = jnp.where(core == 0, split[:, 1], split[:, 0])
    arrived = lax.ppermute(send, "core", [(0, 1), (1, 0)])
    chip_sum = (keep.astype(jnp.float32) + arrived.astype(jnp.float32)).astype(jnp.bfloat16)
    pieces = lax.all_to_all(chip_sum, "rchip", 0, 0)
    return jnp.sum(pieces.astype(jnp.float32), axis=0)


def adjoint_sweep(state_grad, rate_rows, onehot, seq_count):
    channels = state_grad.shape[0]
    seq_rate = jnp.dot(onehot, rate_rows, precision=exact_mode)
    decays = (1.0 - seq_rate).T
    running = state_grad.reshape(channels, seq_count, -1)
    bins = running.shape[2]
    factor = decays[:, :, None]
    shift = 1
    while shift < bins:
        ahead = jnp.concatenate(
            [running[:, :, shift:], jnp.zeros((channels, seq_count, shift), running.dtype)], axis=2
        )
        running = running + factor * ahead
        factor = factor * factor
        shift *= 2
    return running.reshape(channels, -1)


def rate_term(adjoint, states_share, onehot, seq_count):
    channels = adjoint.shape[0]
    adjoint_seq = adjoint.reshape(channels, seq_count, -1)
    previous = states_share.astype(jnp.float32).reshape(channels, seq_count, -1)
    per_seq = jnp.sum(adjoint_seq[:, :, 1:] * previous[:, :, :-1], axis=2)
    return -jnp.dot(onehot.T, per_seq.T, precision=exact_mode)


def per_device(inputs, out_grad, states, in_weight, out_weight, decay_rate, session_ids, lengths):
    n_col = lax.axis_size("col")
    seq_count = session_ids.shape[0]
    onehot = session_table(session_ids, decay_rate.shape[0])
    grad_rows = gather_rows(out_grad, "col", n_col)
    token_total = grad_rows.shape[0]
    bin_count = token_total // seq_count
    token_ids = jnp.arange(token_total, dtype=jnp.int32)
    seq_match = (token_ids // bin_count)[:, None] == jnp.arange(seq_count, dtype=jnp.int32)[None, :]
    seq_length = jnp.sum(jnp.where(seq_match, lengths[None, :], 0), axis=1)
    valid_bin = token_ids % bin_count >= bin_count - seq_length
    masked = jnp.where(valid_bin[:, None], grad_rows, jnp.zeros_like(grad_rows))
    state_grad = scatter_channels(contract(out_weight, masked, 1, 1).astype(jnp.bfloat16))
    states_rows = swap_cores(lax.all_gather(states, "rchip", axis=0, tiled=True))
    masked_columns = jnp.where(valid_bin[None, :], grad_rows.T, jnp.zeros_like(grad_rows.T))
    out_weight_grad = contract(states_rows, masked_columns, 1, 1).astype(jnp.bfloat16)
    adjoint = adjoint_sweep(state_grad, decay_rate, onehot, seq_count)
    rate_grad = rate_term(adjoint, states, onehot, seq_count)
    gathered, own, rest = gather_channels(adjoint.astype(jnp.bfloat16))
    inputs_held, _ = lax.optimization_barrier((inputs, out_grad))
    input_columns = lax.all_gather(inputs_held.T, "col", axis=1, tiled=True)
    in_weight_grad = contract(input_columns, gathered, 1, 1).astype(jnp.bfloat16)
    core = lax.axis_index("core")
    chips = lax.axis_size("rchip")
    weights = in_weight.reshape((in_weight.shape[0], chips, 2, -1))
    own_weight = jnp.where(core == 0, weights[:, :, 0], weights[:, :, 1]).reshape((in_weight.shape[0], -1))
    rest_weight = jnp.where(core == 0, weights[:, :, 1], weights[:, :, 0]).reshape((in_weight.shape[0], -1))
    partial = (contract(own, own_weight, 0, 1) + contract(rest, rest_weight, 0, 1)).astype(jnp.bfloat16)
    pieces = lax.all_to_all(partial.reshape((n_col, -1) + partial.shape[1:]), "col", 0, 0)
    pieces, in_weight_grad, out_weight_grad = lax.optimization_barrier(
        (pieces, in_weight_grad, out_weight_grad)
    )
    input_grad = jnp.sum(pieces.astype(jnp.float32), axis=0).astype(jnp.bfloat16)
    return (input_grad, in_weight_grad, out_weight_grad, rate_grad)


def solution(mesh):
    row = ("rchip", "core")
    split_mesh = Mesh(
        mesh.devices.reshape(mesh.shape["row"] // 2, 2, mesh.shape["col"]), ("rchip", "core", "col")
    )
    return jax.shard_map(
        per_device,
        mesh=split_mesh,
        in_specs=(
            P("col", row),
            P("col", row),
            P(("col",) + row, None),
            P(row, "col"),
            P("col", row),
            P(None, ("col",) + row),
            P(),
            P(),
        ),
        out_specs=(P("col", row), P(row, "col"), P("col", row), P(None, ("col",) + row)),
        check_vma=False,
    )
```
